512 devices in a mesh: dp: 32 (over y, z_lo, core), seq: 16 (over x, z_hi).
Axes of the slice: x: 4, y: 8, z: 8 (z_hi: 4, z_lo: 2; z = z_hi * 2 + z_lo), core: 2. Of those that a mesh axis runs over, the one named last changes fastest.
Arguments:
- query_rows: bfloat16 [32, 2048, 2048], P('dp', 'seq'), may hold values from -6 to 6
- key_rows: bfloat16 [32, 2048, 2048], P('dp', 'seq'), may hold values from -0.5 to 0.5
- value_rows: bfloat16 [32, 2048, 2048], P('dp', 'seq'), may hold values from -6 to 6
- doc_starts: int32 [32, 2048], P('dp', 'seq'), may hold values 0 or 1
- decay_rates: int32 [16], replicated, may hold values from 1 to 100
- out_gain: float32 [2048], replicated, may hold values from 0.1 to 1.9
- cotangent: bfloat16 [32, 2048, 2048], P('dp', 'seq'), may hold values from -6 to 6
Outputs:
- normed: bfloat16 [32, 2048, 2048], P('dp', 'seq')
- grad_query: bfloat16 [32, 2048, 2048], P('dp', 'seq')
- grad_key: bfloat16 [32, 2048, 2048], P('dp', 'seq')
- grad_value: bfloat16 [32, 2048, 2048], P('dp', 'seq')
- grad_gain: float32 [2048], P('dp')
The draws below stay inside these ranges and needn't reach their ends.
All inputs are finite; a program needn't handle non-finite values. No bound on the sum of `doc_starts` on one device may be relied on, other than what follows from the above.
Results may differ from the reference program's by a relative error of at most 0.00085.
Values may be sent and summed in bfloat16 or wider, within the bound.
No kernel may reach another device: no remote copies, remote signals or barrier semaphores. Data moves between devices by JAX's collectives and lax.ppermute only.
A program may use at most 64 MiB of HBM per device.

```python
import math
import jax
import jax.numpy as jnp
from jax import lax

H = 16
E = 128
TOKENS = 2048
SEQS = 32
HE = 2048


def draw_decay_rates(key, part):
    pick_key, slow_key, middle_key, order_key = jax.random.split(key, 4)
    slow_side = jax.random.randint(pick_key, (H,), 0, 2)
    slow_rates = jax.random.randint(slow_key, (H,), 1, 4)
    middle_rates = jax.random.randint(middle_key, (H,), 4, 13)
    rates = jnp.where(slow_side == 1, slow_rates, middle_rates)
    order = jax.random.permutation(order_key, H)
    rates = jnp.where(order == 0, 1, jnp.where(order == 1, 100, rates))
    return rates.astype(jnp.int32)


def plant(array, own_key, least, top_value):
    dims = array.shape
    place = [jax.random.randint(jax.random.fold_in(own_key, axis), (), 0, dims[axis]) for axis in range(len(dims))]
    array = array.at[tuple(place)].set(least)
    longest = dims.index(max(dims))
    place[longest] = (place[longest] + 1) % dims[longest]
    return array.at[tuple(place)].set(top_value)


def spiked(values, rng, source, target, shards_of, factor):
    def block_of(dim):
        return (jnp.arange(values.shape[dim]) // (values.shape[dim] // shards_of)).reshape((-1,) + (1,) * (values.ndim - 1 - dim))

    near = jax.random.permutation(rng, shards_of)[block_of(target)]
    far = (block_of(target) + shards_of // 2) % shards_of
    return jnp.where((block_of(source) == near) | (block_of(source) == far), factor * values, values)


def block_scale(key, dims, pieces, smallest, largest):
    def one(position, parts):
        steps = jax.random.uniform(jax.random.fold_in(jax.random.fold_in(key, 6), position), (parts,), jnp.float32, smallest / len(pieces), largest / len(pieces))
        return jnp.repeat(jnp.exp(steps), dims[position] // parts).reshape((-1,) + (1,) * (len(dims) - position - 1))

    level = one(*pieces[0])
    for cut in pieces[1:]:
        level = level * one(*cut)
    return level


def bell_draw(key, dims, scale, reach, shards=(), kind=jnp.bfloat16):
    drawn = jax.random.normal(key, dims, jnp.float32) * scale
    if len(shards) > 0:
        drawn = block_scale(key, dims, shards, -0.22, 0.18) * drawn
    return jnp.clip(drawn, min=-reach, max=reach).astype(kind)


def heavy_noise(stream_key, shape, spread, bound, pieces, heavy, kind=jnp.bfloat16):
    drawn = spread * jax.random.normal(stream_key, shape, jnp.float32)
    if pieces:
        drawn = drawn * block_scale(stream_key, shape, pieces, -0.22, 0.18)
    return jnp.clip(spiked(drawn, jax.random.fold_in(stream_key, 3), *heavy), -bound, bound).astype(kind)


def setup_inputs(seed: int = 0) -> dict:
    streams_of = jax.random.split(jax.random.key(seed), 8)
    query_rows = bell_draw(streams_of[0], (SEQS, TOKENS, HE), 1.0, 6.0, ((0, 32), (1, 16)))
    key_rows = bell_draw(streams_of[1], (SEQS, TOKENS, HE), E ** -0.5, 0.5, ((0, 32), (1, 16)))
    value_rows = bell_draw(streams_of[2], (SEQS, TOKENS, HE), 1.0, 6.0, ((0, 32), (1, 16)))
    doc_starts = plant((jax.random.randint(streams_of[3], (SEQS, TOKENS), 0, TOKENS) < 2).astype(jnp.int32), jax.random.fold_in(streams_of[3], 1), 0, 1)
    decay_rates = draw_decay_rates(jax.random.fold_in(streams_of[7], 71), 0)
    out_gain = jnp.clip(1.0 + 0.18 * jax.random.normal(streams_of[5], (HE,), jnp.float32), 0.1, 1.9)
    cotangent = heavy_noise(streams_of[6], (SEQS, TOKENS, HE), 1.0, 6.0, ((0, 32), (1, 16)), (0, 2, 32, 2.75))
    return {"query_rows": query_rows, "key_rows": key_rows, "value_rows": value_rows, "doc_starts": doc_starts, "decay_rates": decay_rates, "out_gain": out_gain, "cotangent": cotangent}


highest = lax.Precision.HIGHEST
epsilon = 1e-05

def block_terms(log_decay, marks):
    length = marks.shape[0]
    counted = jnp.cumsum(marks, dtype=jnp.int32)
    places = jnp.arange(length, dtype=jnp.float32)
    offsets = places[:, None] - places[None, :]
    inside = (counted[:, None] == counted[None, :]) & (offsets >= 0.0)
    weights = jnp.where(inside[None], jnp.exp2(log_decay[:, None, None] * jnp.maximum(offsets, 0.0)[None]), 0.0)
    fresh = (counted == 0).astype(jnp.float32)
    entry = fresh[:, None] * jnp.exp2(log_decay[None, :] * (places[:, None] + 1.0))
    latest = counted[length - 1]
    tail = jnp.where((counted == latest)[:, None], jnp.exp2(log_decay[None, :] * (length - 1.0 - places)[:, None]), 0.0)
    through = (latest == 0).astype(jnp.float32) * jnp.exp2(log_decay * length)
    return (weights, entry, tail, through)

def state_sum(key_block, value_block, tail):
    return jnp.einsum('jhe,jhf->hef', key_block * tail[:, :, None], value_block, precision=highest)

def out_sum(query_block, key_block, value_block, state_in, weights, entry):
    scores = jnp.einsum('ihe,jhe->hij', query_block, key_block, precision=highest) * weights
    inner = jnp.einsum('hij,jhe->ihe', scores, value_block, precision=highest)
    carried = jnp.einsum('ihe,hef->ihf', query_block, state_in, precision=highest)
    return inner + entry[:, :, None] * carried

def one_sequence(query_seq, key_seq, value_seq, marks, log_decay):
    length = query_seq.shape[0]
    block = math.gcd(length, 128)
    count = length // block
    heads = log_decay.shape[0]
    width = query_seq.shape[1] // heads

    def split(rows):
        return rows.reshape(count, block, heads, width)

    def step(state, item):
        query_block, key_block, value_block, mark_block = item
        weights, entry, tail, through = block_terms(log_decay, mark_block)
        outs = out_sum(query_block, key_block, value_block, state, weights, entry)
        renewed = through[:, None, None] * state + state_sum(key_block, value_block, tail)
        return (renewed, outs)
    advance = jax.checkpoint(step)
    start = jnp.zeros((heads, width, width), jnp.float32)
    _, outs = lax.scan(advance, start, (split(query_seq), split(key_seq), split(value_seq), marks.reshape(count, block)))
    return outs.reshape(length, heads * width)

def reference(query_rows, key_rows, value_rows, doc_starts, decay_rates, out_gain, cotangent):
    log_decay = -decay_rates.astype(jnp.float32) / TOKENS

    def layer(query_all, key_all, value_all, gain_vec):

        def per_sequence(item):
            return one_sequence(item[0], item[1], item[2], item[3], log_decay)
        attn = lax.map(per_sequence, (query_all, key_all, value_all, doc_starts))
        scale = lax.rsqrt(lax.optimization_barrier(jnp.mean(attn * attn, axis=-1, keepdims=True)) + epsilon)
        return attn * scale * gain_vec
    unrounded, back = jax.vjp(layer, query_rows.astype(jnp.float32), key_rows.astype(jnp.float32), value_rows.astype(jnp.float32), out_gain)
    grads = back(cotangent.astype(jnp.float32))
    return (unrounded.astype(jnp.bfloat16), grads[0].astype(jnp.bfloat16), grads[1].astype(jnp.bfloat16), grads[2].astype(jnp.bfloat16), grads[3])
```

```python
import math

import jax
import jax.numpy as jnp
from jax import lax
from jax.sharding import PartitionSpec as P

E = 128


highest = lax.Precision.HIGHEST
epsilon = 1e-05


def pack(factor, state):
    heads, width, _ = state.shape
    rows = jnp.broadcast_to(factor[:, None, None], (heads, 8, width))
    return jnp.concatenate([state, rows], axis=1)


def scan_exclusive(factor, state, reverse):
    count = lax.axis_size("seq")
    width = state.shape[1]
    run_factor, run_state = factor, state
    out_factor, out_state = jnp.ones_like(factor), jnp.zeros_like(state)
    distance = 1
    while distance < count:
        if reverse:
            pairs = [(i, i - distance) for i in range(distance, count)]
        else:
            pairs = [(i, i + distance) for i in range(count - distance)]
        got = lax.ppermute(pack(run_factor, run_state), "seq", pairs)
        got_state, got_factor = got[:, :width], got[:, width, 0]
        out_state = out_state + out_factor[:, None, None] * got_state
        out_factor = out_factor * got_factor
        if distance * 2 < count:
            run_state = run_state + run_factor[:, None, None] * got_state
            run_factor = run_factor * got_factor
        distance *= 2
    return out_state


def block_terms(log_decay, marks):
    length = marks.shape[0]
    counted = jnp.cumsum(marks, dtype=jnp.int32)
    places = jnp.arange(length, dtype=jnp.float32)
    offsets = places[:, None] - places[None, :]
    inside = (counted[:, None] == counted[None, :]) & (offsets >= 0.0)
    weights = jnp.where(
        inside[None], jnp.exp2(log_decay[:, None, None] * jnp.maximum(offsets, 0.0)[None]), 0.0
    )
    fresh = (counted == 0).astype(jnp.float32)
    entry = fresh[:, None] * jnp.exp2(log_decay[None, :] * (places[:, None] + 1.0))
    latest = counted[length - 1]
    tail = jnp.where(
        (counted == latest)[:, None],
        jnp.exp2(log_decay[None, :] * (length - 1.0 - places)[:, None]),
        0.0,
    )
    through = (latest == 0).astype(jnp.float32) * jnp.exp2(log_decay * length)
    return (weights, entry, tail, through)


def state_sum(key_block, value_block, tail):
    return jnp.einsum("jhe,jhf->hef", key_block * tail[:, :, None], value_block, precision=highest)


def out_sum(query_block, key_block, value_block, state_in, weights, entry):
    scores = jnp.einsum("ihe,jhe->hij", query_block, key_block, precision=highest) * weights
    inner = jnp.einsum("hij,jhe->ihe", scores, value_block, precision=highest)
    carried = jnp.einsum("ihe,hef->ihf", query_block, state_in, precision=highest)
    return inner + entry[:, :, None] * carried


def run_chain(through, terms, start, backward):

    def advance(accum, item):
        factor, term = item
        return (factor[:, None, None] * accum + term, accum)

    return lax.scan(advance, start, (through, terms), reverse=backward)


def ahead_state(factor, state):
    return scan_exclusive(factor, state, False)


def behind_grad(factor, state):
    return scan_exclusive(factor, state, True)


def forward_local(query_seq, key_seq, value_seq, marks, log_decay, link):
    length, heads, width = query_seq.shape
    block = math.gcd(length, 512)
    count = length // block
    query_blocks = query_seq.astype(jnp.float32).reshape(count, block, heads, width)
    key_blocks = key_seq.astype(jnp.float32).reshape(count, block, heads, width)
    value_blocks = value_seq.astype(jnp.float32).reshape(count, block, heads, width)
    weights, entry, tail, through = jax.vmap(block_terms, (None, 0))(
        log_decay, marks.reshape(count, block)
    )

    def states_of(key_part, value_part):
        return jax.vmap(state_sum)(key_part, value_part, tail)

    states, state_back = jax.vjp(states_of, key_blocks, value_blocks)
    empty = jnp.zeros((heads, width, width), jnp.float32)
    own_state = run_chain(through, states, empty, False)[0]
    own_factor = jnp.prod(through, axis=0)
    device_in = link(own_factor, own_state)
    block_in = run_chain(through, states, device_in, False)[1]

    def outs_of(query_part, key_part, value_part, state_part):
        return jax.vmap(out_sum)(query_part, key_part, value_part, state_part, weights, entry)

    outs, out_back = jax.vjp(outs_of, query_blocks, key_blocks, value_blocks, block_in)
    saved = (through, own_factor, state_back, out_back, block, count)
    return (outs.reshape(length, heads * width), saved)


def backward_local(grad_rows, saved, link, heads, width):
    through, own_factor, state_back, out_back, block, count = saved
    length = grad_rows.shape[0]
    grad_blocks = grad_rows.reshape(count, block, heads, width)
    grad_q_part, grad_k_part, grad_v_part, grad_state = out_back(grad_blocks)
    empty = jnp.zeros((heads, width, width), jnp.float32)
    own_grad = run_chain(through, grad_state, empty, True)[0]
    device_out = link(own_factor, own_grad)
    block_out = run_chain(through, grad_state, device_out, True)[1]
    extra_key, extra_value = state_back(block_out)
    flat = (length, heads * width)
    return (
        grad_q_part.reshape(flat),
        (grad_k_part + extra_key).reshape(flat),
        (grad_v_part + extra_value).reshape(flat),
    )


def normalize(mixed, out_gain, cotangent):

    def apply(attn, gain_vec):
        scale = lax.rsqrt(jnp.mean(attn * attn, axis=-1, keepdims=True) + epsilon)
        return attn * scale * gain_vec

    result, back = jax.vjp(apply, mixed, out_gain)
    grad_out, gain_part = back(cotangent.astype(jnp.float32))
    return (result.astype(jnp.bfloat16), grad_out, gain_part)


def per_device(query_rows, key_rows, value_rows, doc_starts, decay_rates, out_gain, cotangent):
    local_tokens = query_rows.shape[1]
    total = local_tokens * lax.axis_size("seq")
    log_decay = -decay_rates.astype(jnp.float32) / total
    heads = query_rows.shape[2] // E
    shaped = (local_tokens, heads, E)
    outs, saved = forward_local(
        query_rows[0].reshape(shaped),
        key_rows[0].reshape(shaped),
        value_rows[0].reshape(shaped),
        doc_starts[0],
        log_decay,
        ahead_state,
    )
    normed, grad_out, gain_part = normalize(outs[None], out_gain, cotangent)
    grads = backward_local(grad_out[0], saved, behind_grad, heads, E)
    grad_query = grads[0][None].astype(jnp.bfloat16)
    grad_key = grads[1][None].astype(jnp.bfloat16)
    grad_value = grads[2][None].astype(jnp.bfloat16)
    summed = lax.psum(gain_part, ("dp", "seq"))
    share = summed.shape[-1] // lax.axis_size("dp")
    grad_gain = lax.dynamic_slice_in_dim(summed, lax.axis_index("dp") * share, share)
    return (normed, grad_query, grad_key, grad_value, grad_gain)


def solution(mesh):
    return jax.shard_map(
        per_device,
        mesh=mesh,
        in_specs=(
            P("dp", "seq", None),
            P("dp", "seq", None),
            P("dp", "seq", None),
            P("dp", "seq"),
            P(),
            P(),
            P("dp", "seq", None),
        ),
        out_specs=(
            P("dp", "seq", None),
            P("dp", "seq", None),
            P("dp", "seq", None),
            P("dp", "seq", None),
            P("dp"),
        ),
        check_vma=False,
    )
```

```python
import jax
import jax.numpy as jnp
from jax import lax
from jax.sharding import PartitionSpec as P

E = 128
CHUNK = 128


highest = lax.Precision.HIGHEST
epsilon = 1e-05


def block_terms(log_decay, marks):
    length = marks.shape[0]
    counted = jnp.cumsum(marks, dtype=jnp.int32)
    places = jnp.arange(length, dtype=jnp.float32)
    offsets = places[:, None] - places[None, :]
    inside = (counted[:, None] == counted[None, :]) & (offsets >= 0.0)
    weights = jnp.where(
        inside[None], jnp.exp2(log_decay[:, None, None] * jnp.maximum(offsets, 0.0)[None]), 0.0
    )
    fresh = (counted == 0).astype(jnp.float32)
    entry = fresh[:, None] * jnp.exp2(log_decay[None, :] * (places[:, None] + 1.0))
    latest = counted[length - 1]
    tail = jnp.where(
        (counted == latest)[:, None],
        jnp.exp2(log_decay[None, :] * (length - 1.0 - places)[:, None]),
        0.0,
    )
    return (weights, entry, tail)


def state_sum(key_block, value_block, tail):
    return jnp.einsum("jhe,jhf->hef", key_block * tail[:, :, None], value_block, precision=highest)


def out_sum(query_block, key_block, value_block, state_in, weights, entry):
    scores = jnp.einsum("ihe,jhe->hij", query_block, key_block, precision=highest) * weights
    inner = jnp.einsum("hij,jhe->ihe", scores, value_block, precision=highest)
    carried = jnp.einsum("ihe,hef->ihf", query_block, state_in, precision=highest)
    return inner + entry[:, :, None] * carried


def chunk_mixing(log_decay, marks, count, length):
    starts = jnp.cumsum(jnp.sum(marks.reshape(count, length), axis=1), dtype=jnp.int32)
    chunk = jnp.arange(count)
    before = jnp.where(chunk >= 1, starts[jnp.maximum(chunk - 1, 0)], 0)
    clear = (chunk[None, :] < chunk[:, None]) & (before[:, None] - starts[None, :] == 0)
    gap = jnp.maximum(chunk[:, None] - chunk[None, :] - 1, 0).astype(jnp.float32)
    return jnp.where(clear[None], jnp.exp2(log_decay[:, None, None] * (length * gap)[None]), 0.0)


def local_attention(query_seq, key_seq, value_seq, marks, log_decay):
    tokens, heads, width = query_seq.shape
    length = CHUNK
    count = tokens // length

    def split(rows):
        return rows.reshape(count, length, heads, width)

    query_blocks, key_blocks, value_blocks = split(query_seq), split(key_seq), split(value_seq)
    weights, entry, tail = jax.vmap(block_terms, (None, 0))(log_decay, marks.reshape(count, length))
    states = jax.vmap(state_sum)(key_blocks, value_blocks, tail)
    mixing = chunk_mixing(log_decay, marks, count, length)
    block_in = jnp.einsum("hcd,dhef->chef", mixing, states, precision=highest)
    outs = jax.vmap(out_sum)(query_blocks, key_blocks, value_blocks, block_in, weights, entry)
    return outs.reshape(tokens, heads * width)


def per_device(query_rows, key_rows, value_rows, doc_starts, decay_rates, out_gain, cotangent):
    count = lax.axis_size("seq")
    place = lax.axis_index("seq")
    local_tokens, features = query_rows.shape[1], query_rows.shape[2]
    tokens = local_tokens * count
    heads = features // E // count
    width = heads * E
    log_decay = lax.dynamic_slice_in_dim(-decay_rates.astype(jnp.float32) / tokens, place * heads, heads)
    gain = lax.dynamic_slice_in_dim(out_gain, place * width, width)

    stacked = jnp.stack([query_rows[0], key_rows[0], value_rows[0], cotangent[0]])
    stacked = stacked.reshape(4, local_tokens, count, width)
    moved = lax.all_to_all(stacked, "seq", 2, 1, tiled=True).reshape(4, tokens, heads, E)
    marks = lax.all_gather(doc_starts[0], "seq", tiled=True)

    query_seq, key_seq, value_seq = (moved[i].astype(jnp.float32) for i in range(3))
    grad_rows = moved[3].astype(jnp.float32).reshape(tokens, width)
    attn, back = jax.vjp(
        lambda q, k, v: local_attention(q, k, v, marks, log_decay), query_seq, key_seq, value_seq
    )
    stats = jnp.stack([jnp.sum(attn * attn, axis=-1), jnp.sum(attn * gain * grad_rows, axis=-1)])
    totals = lax.psum(stats, "seq")
    scale = lax.rsqrt(totals[0] / features + epsilon)[:, None]
    normed = attn * scale * gain
    grad_attn = gain * grad_rows * scale - attn * (scale**3 * (totals[1] / features)[:, None])
    gain_part = jnp.sum(grad_rows * attn * scale, axis=0)
    grad_q, grad_k, grad_v = back(grad_attn)

    outs = jnp.stack(
        [normed, grad_q.reshape(tokens, width), grad_k.reshape(tokens, width), grad_v.reshape(tokens, width)]
    ).astype(jnp.bfloat16)
    outs = outs.reshape(4, count, local_tokens, width)
    returned = lax.all_to_all(outs, "seq", 1, 3, tiled=True).reshape(4, 1, local_tokens, features)

    gain_seq = jnp.sum(lax.all_gather(gain_part, "dp"), axis=0)
    gain_all = lax.all_gather(gain_seq, "seq", tiled=True)
    share = features // lax.axis_size("dp")
    grad_gain = lax.dynamic_slice_in_dim(gain_all, lax.axis_index("dp") * share, share)
    return (returned[0], returned[1], returned[2], returned[3], grad_gain)


def solution(mesh):
    return jax.shard_map(
        per_device,
        mesh=mesh,
        in_specs=(
            P("dp", "seq", None),
            P("dp", "seq", None),
            P("dp", "seq", None),
            P("dp", "seq"),
            P(),
            P(),
            P("dp", "seq", None),
        ),
        out_specs=(
            P("dp", "seq", None),
            P("dp", "seq", None),
            P("dp", "seq", None),
            P("dp", "seq", None),
            P("dp"),
        ),
        check_vma=False,
    )
```

```python
import jax
import jax.numpy as jnp
from jax import lax
from jax.sharding import PartitionSpec as P

E = 128
CHUNK = 128


highest = lax.Precision.HIGHEST
epsilon = 1e-05


def block_terms(log_decay, marks):
    length = marks.shape[0]
    counted = jnp.cumsum(marks, dtype=jnp.int32)
    places = jnp.arange(length, dtype=jnp.float32)
    offsets = places[:, None] - places[None, :]
    inside = (counted[:, None] == counted[None, :]) & (offsets >= 0.0)
    weights = jnp.where(
        inside[None], jnp.exp2(log_decay[:, None, None] * jnp.maximum(offsets, 0.0)[None]), 0.0
    )
    fresh = (counted == 0).astype(jnp.float32)
    entry = fresh[:, None] * jnp.exp2(log_decay[None, :] * (places[:, None] + 1.0))
    latest = counted[length - 1]
    tail = jnp.where(
        (counted == latest)[:, None],
        jnp.exp2(log_decay[None, :] * (length - 1.0 - places)[:, None]),
        0.0,
    )
    return (weights, entry, tail)


def state_sum(key_block, value_block, tail):
    return jnp.einsum("jhe,jhf->hef", key_block * tail[:, :, None], value_block, precision=highest)


def out_sum(query_block, key_block, value_block, state_in, weights, entry):
    scores = jnp.einsum("ihe,jhe->hij", query_block, key_block, precision=highest) * weights
    inner = jnp.einsum("hij,jhe->ihe", scores, value_block, precision=highest)
    carried = jnp.einsum("ihe,hef->ihf", query_block, state_in, precision=highest)
    return inner + entry[:, :, None] * carried


def chunk_mixing(log_decay, marks, count, length):
    starts = jnp.cumsum(jnp.sum(marks.reshape(count, length), axis=1), dtype=jnp.int32)
    chunk = jnp.arange(count)
    before = jnp.where(chunk >= 1, starts[jnp.maximum(chunk - 1, 0)], 0)
    clear = (chunk[None, :] < chunk[:, None]) & (before[:, None] - starts[None, :] == 0)
    gap = jnp.maximum(chunk[:, None] - chunk[None, :] - 1, 0).astype(jnp.float32)
    return jnp.where(clear[None], jnp.exp2(log_decay[:, None, None] * (length * gap)[None]), 0.0)


def local_attention(query_seq, key_seq, value_seq, marks, log_decay):
    tokens, heads, width = query_seq.shape
    length = CHUNK
    count = tokens // length

    def split(rows):
        return rows.reshape(count, length, heads, width)

    query_blocks, key_blocks, value_blocks = split(query_seq), split(key_seq), split(value_seq)
    weights, entry, tail = jax.vmap(block_terms, (None, 0))(log_decay, marks.reshape(count, length))
    states = jax.vmap(state_sum)(key_blocks, value_blocks, tail)
    mixing = chunk_mixing(log_decay, marks, count, length)
    block_in = jnp.einsum("hcd,dhef->chef", mixing, states, precision=highest)
    outs = jax.vmap(out_sum)(query_blocks, key_blocks, value_blocks, block_in, weights, entry)
    return outs.reshape(tokens, heads * width)


def butterfly_sum(part, axis):
    count = lax.axis_size(axis)
    if count & (count - 1):
        return lax.psum(part, axis)
    distance = 1
    while distance < count:
        part = part + lax.ppermute(part, axis, [(i, i ^ distance) for i in range(count)])
        distance *= 2
    return part


def exact_pieces(values):
    pieces = []
    rest = values
    for _ in range(3):
        piece = lax.reduce_precision(rest, exponent_bits=8, mantissa_bits=7)
        pieces.append(piece)
        rest = rest - piece
    return jnp.stack(pieces).astype(jnp.bfloat16)


def per_device(query_rows, key_rows, value_rows, doc_starts, decay_rates, out_gain, cotangent):
    count = lax.axis_size("seq")
    place = lax.axis_index("seq")
    local_tokens, features = query_rows.shape[1], query_rows.shape[2]
    tokens = local_tokens * count
    heads = features // E // count
    width = heads * E
    log_decay = lax.dynamic_slice_in_dim(-decay_rates.astype(jnp.float32) / tokens, place * heads, heads)
    gain = lax.dynamic_slice_in_dim(out_gain, place * width, width)

    mark_rows = local_tokens // width
    extra = -(-max(mark_rows, 1) // 8) * 8
    stacked = jnp.stack([query_rows[0], key_rows[0], value_rows[0], cotangent[0]])
    stacked = stacked.reshape(4, local_tokens, count, width)
    side = jnp.zeros((4, extra, count, width), jnp.bfloat16)
    side = side.at[0, :mark_rows].set(
        jnp.broadcast_to(doc_starts[0].astype(jnp.bfloat16).reshape(mark_rows, 1, width), (mark_rows, count, width))
    )
    moved = lax.all_to_all(jnp.concatenate([stacked, side], axis=1), "seq", 2, 1, tiled=True)
    moved = moved.reshape(4, count, local_tokens + extra, width)
    marks = moved[0, :, local_tokens:local_tokens + mark_rows].reshape(tokens).astype(jnp.int32)
    moved = moved[:, :, :local_tokens].reshape(4, tokens, heads, E)

    query_seq, key_seq, value_seq = (moved[i].astype(jnp.float32) for i in range(3))
    grad_rows = moved[3].astype(jnp.float32).reshape(tokens, width)
    attn, back = jax.vjp(
        lambda q, k, v: local_attention(q, k, v, marks, log_decay), query_seq, key_seq, value_seq
    )
    stats = jnp.stack([jnp.sum(attn * attn, axis=-1), jnp.sum(attn * gain * grad_rows, axis=-1)])
    totals = butterfly_sum(stats, "seq")
    scale = lax.rsqrt(totals[0] / features + epsilon)[:, None]
    normed = attn * scale * gain
    grad_attn = gain * grad_rows * scale - attn * (scale**3 * (totals[1] / features)[:, None])
    gain_part = jnp.sum(grad_rows * attn * scale, axis=0)
    gain_total = butterfly_sum(gain_part, "dp")
    grad_q, grad_k, grad_v = back(grad_attn)

    outs = jnp.stack(
        [normed, grad_q.reshape(tokens, width), grad_k.reshape(tokens, width), grad_v.reshape(tokens, width)]
    ).astype(jnp.bfloat16)
    outs = outs.reshape(4, count, local_tokens, width)
    tail = jnp.zeros((4, count, 8, width), jnp.bfloat16)
    tail = tail.at[:3, :, 0].set(jnp.broadcast_to(exact_pieces(gain_total)[:, None], (3, count, width)))
    returned = lax.all_to_all(jnp.concatenate([outs, tail], axis=2), "seq", 1, 3, tiled=True)
    returned = returned.reshape(4, local_tokens + 8, features)
    gain_all = jnp.sum(returned[:3, local_tokens].astype(jnp.float32), axis=0)
    share = features // lax.axis_size("dp")
    grad_gain = lax.dynamic_slice_in_dim(gain_all, lax.axis_index("dp") * share, share)
    results = returned[:, None, :local_tokens]
    return (results[0], results[1], results[2], results[3], grad_gain)


def solution(mesh):
    return jax.shard_map(
        per_device,
        mesh=mesh,
        in_specs=(
            P("dp", "seq", None),
            P("dp", "seq", None),
            P("dp", "seq", None),
            P("dp", "seq"),
            P(),
            P(),
            P("dp", "seq", None),
        ),
        out_specs=(
            P("dp", "seq", None),
            P("dp", "seq", None),
            P("dp", "seq", None),
            P("dp", "seq", None),
            P("dp"),
        ),
        check_vma=False,
    )
```

```python
import jax
import jax.numpy as jnp
from jax import lax
from jax.sharding import PartitionSpec as P

E = 128
CHUNK = 128


highest = lax.Precision.HIGHEST
epsilon = 1e-05


def block_terms(log_decay, marks):
    length = marks.shape[0]
    counted = jnp.cumsum(marks, dtype=jnp.int32)
    places = jnp.arange(length, dtype=jnp.float32)
    offsets = places[:, None] - places[None, :]
    inside = (counted[:, None] == counted[None, :]) & (offsets >= 0.0)
    weights = jnp.where(
        inside[None], jnp.exp2(log_decay[:, None, None] * jnp.maximum(offsets, 0.0)[None]), 0.0
    )
    fresh = (counted == 0).astype(jnp.float32)
    entry = fresh[:, None] * jnp.exp2(log_decay[None, :] * (places[:, None] + 1.0))
    latest = counted[length - 1]
    tail = jnp.where(
        (counted == latest)[:, None],
        jnp.exp2(log_decay[None, :] * (length - 1.0 - places)[:, None]),
        0.0,
    )
    return (weights, entry, tail)


def state_sum(key_block, value_block, tail):
    return jnp.einsum("jhe,jhf->hef", key_block * tail[:, :, None], value_block, precision=highest)


def out_sum(query_block, key_block, value_block, state_in, weights, entry):
    scores = jnp.einsum("ihe,jhe->hij", query_block, key_block, precision=highest) * weights
    inner = jnp.einsum("hij,jhe->ihe", scores, value_block, precision=highest)
    carried = jnp.einsum("ihe,hef->ihf", query_block, state_in, precision=highest)
    return inner + entry[:, :, None] * carried


def chunk_mixing(log_decay, marks, count, length):
    starts = jnp.cumsum(jnp.sum(marks.reshape(count, length), axis=1), dtype=jnp.int32)
    chunk = jnp.arange(count)
    before = jnp.where(chunk >= 1, starts[jnp.maximum(chunk - 1, 0)], 0)
    clear = (chunk[None, :] < chunk[:, None]) & (before[:, None] - starts[None, :] == 0)
    gap = jnp.maximum(chunk[:, None] - chunk[None, :] - 1, 0).astype(jnp.float32)
    return jnp.where(clear[None], jnp.exp2(log_decay[:, None, None] * (length * gap)[None]), 0.0)


def local_attention(query_seq, key_seq, value_seq, marks, log_decay):
    tokens, heads, width = query_seq.shape
    length = CHUNK
    count = tokens // length

    def split(rows):
        return rows.reshape(count, length, heads, width)

    query_blocks, key_blocks, value_blocks = split(query_seq), split(key_seq), split(value_seq)
    weights, entry, tail = jax.vmap(block_terms, (None, 0))(log_decay, marks.reshape(count, length))
    states = jax.vmap(state_sum)(key_blocks, value_blocks, tail)
    mixing = chunk_mixing(log_decay, marks, count, length)
    block_in = jnp.einsum("hcd,dhef->chef", mixing, states, precision=highest)
    outs = jax.vmap(out_sum)(query_blocks, key_blocks, value_blocks, block_in, weights, entry)
    return outs.reshape(tokens, heads * width)


def butterfly_sum(part, axis):
    count = lax.axis_size(axis)
    if count & (count - 1):
        return lax.psum(part, axis)
    distance = 1
    while distance < count:
        part = part + lax.ppermute(part, axis, [(i, i ^ distance) for i in range(count)])
        distance *= 2
    return part


def exact_pieces(values):
    pieces = []
    rest = values
    for _ in range(3):
        piece = lax.reduce_precision(rest, exponent_bits=8, mantissa_bits=7)
        pieces.append(piece)
        rest = rest - piece
    return jnp.stack(pieces).astype(jnp.bfloat16)


def per_device(query_rows, key_rows, value_rows, doc_starts, decay_rates, out_gain, cotangent):
    count = lax.axis_size("seq")
    place = lax.axis_index("seq")
    local_tokens, features = query_rows.shape[1], query_rows.shape[2]
    tokens = local_tokens * count
    heads = features // E // count
    width = heads * E
    log_decay = lax.dynamic_slice_in_dim(-decay_rates.astype(jnp.float32) / tokens, place * heads, heads)
    gain = lax.dynamic_slice_in_dim(out_gain, place * width, width)

    mark_rows = local_tokens // width
    extra = -(-max(mark_rows, 1) // 8) * 8
    side = jnp.zeros((count, extra, width), jnp.bfloat16)
    side = side.at[:, :mark_rows].set(
        jnp.broadcast_to(doc_starts[0].astype(jnp.bfloat16).reshape(1, mark_rows, width), (count, mark_rows, width))
    )
    pieces = [rows[0].reshape(local_tokens, count, width).transpose(1, 0, 2)
              for rows in (query_rows, key_rows, value_rows, cotangent)]
    moved = lax.all_to_all(jnp.concatenate(pieces + [side], axis=1), "seq", 0, 0, tiled=True)
    span = 4 * local_tokens
    marks = moved[:, span:span + mark_rows].reshape(tokens).astype(jnp.int32)
    moved = moved[:, :span].reshape(count, 4, local_tokens, heads, E).transpose(1, 0, 2, 3, 4)
    moved = moved.reshape(4, tokens, heads, E)

    query_seq, key_seq, value_seq = (moved[i].astype(jnp.float32) for i in range(3))
    grad_rows = moved[3].astype(jnp.float32).reshape(tokens, width)
    attn, back = jax.vjp(
        lambda q, k, v: local_attention(q, k, v, marks, log_decay), query_seq, key_seq, value_seq
    )
    stats = jnp.stack([jnp.sum(attn * attn, axis=-1), jnp.sum(attn * gain * grad_rows, axis=-1)])
    totals = butterfly_sum(stats, "seq")
    scale = lax.rsqrt(totals[0] / features + epsilon)[:, None]
    normed = attn * scale * gain
    grad_attn = gain * grad_rows * scale - attn * (scale**3 * (totals[1] / features)[:, None])
    gain_part = jnp.sum(grad_rows * attn * scale, axis=0)
    gain_total = butterfly_sum(gain_part, "dp")
    grad_q, grad_k, grad_v = back(grad_attn)

    outs = [part.reshape(count, local_tokens, width).astype(jnp.bfloat16)
            for part in (normed, grad_q, grad_k, grad_v)]
    tail = jnp.zeros((count, 8, width), jnp.bfloat16)
    tail = tail.at[:, :3].set(jnp.broadcast_to(exact_pieces(gain_total)[None], (count, 3, width)))
    returned = lax.all_to_all(jnp.concatenate(outs + [tail], axis=1), "seq", 0, 0, tiled=True)
    span = 4 * local_tokens
    gain_all = jnp.sum(returned[:, span:span + 3].astype(jnp.float32), axis=1).reshape(features)
    results = returned[:, :span].reshape(count, 4, local_tokens, width).transpose(1, 2, 0, 3)
    results = results.reshape(4, 1, local_tokens, features)
    share = features // lax.axis_size("dp")
    grad_gain = lax.dynamic_slice_in_dim(gain_all, lax.axis_index("dp") * share, share)
    return (results[0], results[1], results[2], results[3], grad_gain)


def solution(mesh):
    return jax.shard_map(
        per_device,
        mesh=mesh,
        in_specs=(
            P("dp", "seq", None),
            P("dp", "seq", None),
            P("dp", "seq", None),
            P("dp", "seq"),
            P(),
            P(),
            P("dp", "seq", None),
        ),
        out_specs=(
            P("dp", "seq", None),
            P("dp", "seq", None),
            P("dp", "seq", None),
            P("dp", "seq", None),
            P("dp"),
        ),
        check_vma=False,
    )
```

```python
import jax
import jax.numpy as jnp
from jax import lax
from jax.sharding import PartitionSpec as P

E = 128
CHUNK = 128


highest = lax.Precision.HIGHEST
epsilon = 1e-05


def block_terms(log_decay, marks):
    length = marks.shape[0]
    counted = jnp.cumsum(marks, dtype=jnp.int32)
    places = jnp.arange(length, dtype=jnp.float32)
    offsets = places[:, None] - places[None, :]
    inside = (counted[:, None] == counted[None, :]) & (offsets >= 0.0)
    weights = jnp.where(
        inside[None], jnp.exp2(log_decay[:, None, None] * jnp.maximum(offsets, 0.0)[None]), 0.0
    )
    fresh = (counted == 0).astype(jnp.float32)
    entry = fresh[:, None] * jnp.exp2(log_decay[None, :] * (places[:, None] + 1.0))
    latest = counted[length - 1]
    tail = jnp.where(
        (counted == latest)[:, None],
        jnp.exp2(log_decay[None, :] * (length - 1.0 - places)[:, None]),
        0.0,
    )
    return (weights, entry, tail)


def state_sum(key_block, value_block, tail):
    return jnp.einsum("jhe,jhf->hef", key_block * tail[:, :, None], value_block, precision=highest)


def out_sum(query_block, key_block, value_block, state_in, weights, entry):
    scores = jnp.einsum("ihe,jhe->hij", query_block, key_block, precision=highest) * weights
    inner = jnp.einsum("hij,jhe->ihe", scores, value_block, precision=highest)
    carried = jnp.einsum("ihe,hef->ihf", query_block, state_in, precision=highest)
    return inner + entry[:, :, None] * carried


def chunk_mixing(log_decay, marks, count, length):
    starts = jnp.cumsum(jnp.sum(marks.reshape(count, length), axis=1), dtype=jnp.int32)
    chunk = jnp.arange(count)
    before = jnp.where(chunk >= 1, starts[jnp.maximum(chunk - 1, 0)], 0)
    clear = (chunk[None, :] < chunk[:, None]) & (before[:, None] - starts[None, :] == 0)
    gap = jnp.maximum(chunk[:, None] - chunk[None, :] - 1, 0).astype(jnp.float32)
    return jnp.where(clear[None], jnp.exp2(log_decay[:, None, None] * (length * gap)[None]), 0.0)


def local_attention(query_seq, key_seq, value_seq, marks, log_decay):
    tokens, heads, width = query_seq.shape
    length = CHUNK
    count = tokens // length

    def split(rows):
        return rows.reshape(count, length, heads, width)

    query_blocks, key_blocks, value_blocks = split(query_seq), split(key_seq), split(value_seq)
    weights, entry, tail = jax.vmap(block_terms, (None, 0))(log_decay, marks.reshape(count, length))
    states = jax.vmap(state_sum)(key_blocks, value_blocks, tail)
    mixing = chunk_mixing(log_decay, marks, count, length)
    block_in = jnp.einsum("hcd,dhef->chef", mixing, states, precision=highest)
    outs = jax.vmap(out_sum)(query_blocks, key_blocks, value_blocks, block_in, weights, entry)
    return outs.reshape(tokens, heads * width)


def butterfly_sum(part, axis):
    count = lax.axis_size(axis)
    if count & (count - 1):
        return lax.psum(part, axis)
    distance = 1
    while distance < count:
        part = part + lax.ppermute(part, axis, [(i, i ^ distance) for i in range(count)])
        distance *= 2
    return part


def token_sum(stats, count):
    kinds, tokens = stats.shape
    blocks = stats.reshape(kinds, count, tokens // count).transpose(1, 0, 2)
    own = jnp.sum(lax.all_to_all(blocks, "seq", 0, 0, tiled=True), axis=0)
    spread = jnp.broadcast_to(own[None], (count,) + own.shape)
    gathered = lax.all_to_all(spread, "seq", 0, 0, tiled=True)
    return gathered.transpose(1, 0, 2).reshape(kinds, tokens)


def exact_pieces(values):
    pieces = []
    rest = values
    for _ in range(3):
        piece = lax.reduce_precision(rest, exponent_bits=8, mantissa_bits=7)
        pieces.append(piece)
        rest = rest - piece
    return jnp.stack(pieces).astype(jnp.bfloat16)


def per_device(query_rows, key_rows, value_rows, doc_starts, decay_rates, out_gain, cotangent):
    count = lax.axis_size("seq")
    place = lax.axis_index("seq")
    local_tokens, features = query_rows.shape[1], query_rows.shape[2]
    tokens = local_tokens * count
    heads = features // E // count
    width = heads * E
    log_decay = lax.dynamic_slice_in_dim(-decay_rates.astype(jnp.float32) / tokens, place * heads, heads)
    gain = lax.dynamic_slice_in_dim(out_gain, place * width, width)

    mark_rows = local_tokens // width
    extra = -(-max(mark_rows, 1) // 8) * 8
    side = jnp.zeros((count, extra, width), jnp.bfloat16)
    side = side.at[:, :mark_rows].set(
        jnp.broadcast_to(doc_starts[0].astype(jnp.bfloat16).reshape(1, mark_rows, width), (count, mark_rows, width))
    )
    pieces = [rows[0].reshape(local_tokens, count, width).transpose(1, 0, 2)
              for rows in (query_rows, key_rows, value_rows, cotangent)]
    moved = lax.all_to_all(jnp.concatenate(pieces + [side], axis=1), "seq", 0, 0, tiled=True)
    span = 4 * local_tokens
    marks = moved[:, span:span + mark_rows].reshape(tokens).astype(jnp.int32)
    moved = moved[:, :span].reshape(count, 4, local_tokens, heads, E).transpose(1, 0, 2, 3, 4)
    moved = moved.reshape(4, tokens, heads, E)

    query_seq, key_seq, value_seq = (moved[i].astype(jnp.float32) for i in range(3))
    grad_rows = moved[3].astype(jnp.float32).reshape(tokens, width)
    attn, back = jax.vjp(
        lambda q, k, v: local_attention(q, k, v, marks, log_decay), query_seq, key_seq, value_seq
    )
    stats = jnp.stack([jnp.sum(attn * attn, axis=-1), jnp.sum(attn * gain * grad_rows, axis=-1)])
    totals = token_sum(stats, count)
    scale = lax.rsqrt(totals[0] / features + epsilon)[:, None]
    normed = attn * scale * gain
    grad_attn = gain * grad_rows * scale - attn * (scale**3 * (totals[1] / features)[:, None])
    gain_part = jnp.sum(grad_rows * attn * scale, axis=0)
    grad_q, grad_k, grad_v = back(grad_attn)

    outs = [part.reshape(count, local_tokens, width).astype(jnp.bfloat16)
            for part in (normed, grad_q, grad_k, grad_v)]
    tail = jnp.zeros((count, 8, width), jnp.bfloat16)
    tail = tail.at[:, :3].set(jnp.broadcast_to(exact_pieces(gain_part)[None], (count, 3, width)))
    returned = lax.all_to_all(jnp.concatenate(outs + [tail], axis=1), "seq", 0, 0, tiled=True)
    span = 4 * local_tokens
    gain_all = jnp.sum(returned[:, span:span + 3].astype(jnp.float32), axis=1).reshape(features)
    results = returned[:, :span].reshape(count, 4, local_tokens, width).transpose(1, 2, 0, 3)
    results = results.reshape(4, 1, local_tokens, features)
    groups = lax.axis_size("dp")
    spread = lax.all_to_all(gain_all.reshape(groups, features // groups), "dp", 0, 0, tiled=True)
    grad_gain = jnp.sum(spread, axis=0)
    return (results[0], results[1], results[2], results[3], grad_gain)


def solution(mesh):
    return jax.shard_map(
        per_device,
        mesh=mesh,
        in_specs=(
            P("dp", "seq", None),
            P("dp", "seq", None),
            P("dp", "seq", None),
            P("dp", "seq"),
            P(),
            P(),
            P("dp", "seq", None),
        ),
        out_specs=(
            P("dp", "seq", None),
            P("dp", "seq", None),
            P("dp", "seq", None),
            P("dp", "seq", None),
            P("dp"),
        ),
        check_vma=False,
    )
```

```python
import jax
import jax.numpy as jnp
from jax import lax
from jax.sharding import PartitionSpec as P

E = 128
CHUNK = 128


highest = lax.Precision.HIGHEST
epsilon = 1e-05


def block_terms(log_decay, marks):
    length = marks.shape[0]
    counted = jnp.cumsum(marks, dtype=jnp.int32)
    places = jnp.arange(length, dtype=jnp.float32)
    offsets = places[:, None] - places[None, :]
    inside = (counted[:, None] == counted[None, :]) & (offsets >= 0.0)
    weights = jnp.where(
        inside[None], jnp.exp2(log_decay[:, None, None] * jnp.maximum(offsets, 0.0)[None]), 0.0
    )
    fresh = (counted == 0).astype(jnp.float32)
    entry = fresh[:, None] * jnp.exp2(log_decay[None, :] * (places[:, None] + 1.0))
    latest = counted[length - 1]
    tail = jnp.where(
        (counted == latest)[:, None],
        jnp.exp2(log_decay[None, :] * (length - 1.0 - places)[:, None]),
        0.0,
    )
    return (weights, entry, tail)


def state_sum(key_block, value_block, tail):
    return jnp.einsum("jhe,jhf->hef", key_block * tail[:, :, None], value_block, precision=highest)


def out_sum(query_block, key_block, value_block, state_in, weights, entry):
    scores = jnp.einsum("ihe,jhe->hij", query_block, key_block, precision=highest) * weights
    inner = jnp.einsum("hij,jhe->ihe", scores, value_block, precision=highest)
    carried = jnp.einsum("ihe,hef->ihf", query_block, state_in, precision=highest)
    return inner + entry[:, :, None] * carried


def chunk_mixing(log_decay, marks, count, length):
    starts = jnp.cumsum(jnp.sum(marks.reshape(count, length), axis=1), dtype=jnp.int32)
    chunk = jnp.arange(count)
    before = jnp.where(chunk >= 1, starts[jnp.maximum(chunk - 1, 0)], 0)
    clear = (chunk[None, :] < chunk[:, None]) & (before[:, None] - starts[None, :] == 0)
    gap = jnp.maximum(chunk[:, None] - chunk[None, :] - 1, 0).astype(jnp.float32)
    return jnp.where(clear[None], jnp.exp2(log_decay[:, None, None] * (length * gap)[None]), 0.0)


def local_attention(query_seq, key_seq, value_seq, marks, log_decay):
    tokens, heads, width = query_seq.shape
    length = CHUNK
    count = tokens // length

    def split(rows):
        return rows.reshape(count, length, heads, width)

    query_blocks, key_blocks, value_blocks = split(query_seq), split(key_seq), split(value_seq)
    weights, entry, tail = jax.vmap(block_terms, (None, 0))(log_decay, marks.reshape(count, length))
    states = jax.vmap(state_sum)(key_blocks, value_blocks, tail)
    mixing = chunk_mixing(log_decay, marks, count, length)
    block_in = jnp.einsum("hcd,dhef->chef", mixing, states, precision=highest)
    outs = jax.vmap(out_sum)(query_blocks, key_blocks, value_blocks, block_in, weights, entry)
    return outs.reshape(tokens, heads * width)


def butterfly_sum(part, axis):
    count = lax.axis_size(axis)
    if count & (count - 1):
        return lax.psum(part, axis)
    distance = 1
    while distance < count:
        part = part + lax.ppermute(part, axis, [(i, i ^ distance) for i in range(count)])
        distance *= 2
    return part


def gathered_sum(part, axis):
    count = lax.axis_size(axis)
    spread = jnp.broadcast_to(part[None], (count,) + part.shape)
    return jnp.sum(lax.all_to_all(spread, axis, 0, 0, tiled=True), axis=0)


def exact_pieces(values):
    pieces = []
    rest = values
    for _ in range(3):
        piece = lax.reduce_precision(rest, exponent_bits=8, mantissa_bits=7)
        pieces.append(piece)
        rest = rest - piece
    return jnp.stack(pieces).astype(jnp.bfloat16)


def per_device(query_rows, key_rows, value_rows, doc_starts, decay_rates, out_gain, cotangent):
    count = lax.axis_size("seq")
    place = lax.axis_index("seq")
    local_tokens, features = query_rows.shape[1], query_rows.shape[2]
    tokens = local_tokens * count
    heads = features // E // count
    width = heads * E
    mark_rows = local_tokens // width
    extra = -(-max(mark_rows, 1) // 8) * 8
    side = jnp.zeros((count, extra, width), jnp.bfloat16)
    side = side.at[:, :mark_rows].set(
        jnp.broadcast_to(doc_starts[0].astype(jnp.bfloat16).reshape(1, mark_rows, width), (count, mark_rows, width))
    )
    pieces = [rows[0].reshape(local_tokens, count, width).transpose(1, 0, 2)
              for rows in (query_rows, key_rows, value_rows, cotangent)]
    moved = lax.all_to_all(jnp.concatenate(pieces + [side], axis=1), "seq", 0, 0, tiled=True)
    moved, decay_rates, out_gain = lax.optimization_barrier((moved, decay_rates, out_gain))
    span = 4 * local_tokens
    marks = moved[:, span:span + mark_rows].reshape(tokens).astype(jnp.int32)
    moved = moved[:, :span].reshape(count, 4, local_tokens, heads, E).transpose(1, 0, 2, 3, 4)
    moved = moved.reshape(4, tokens, heads, E)
    log_decay = lax.dynamic_slice_in_dim(-decay_rates.astype(jnp.float32) / tokens, place * heads, heads)
    gain = lax.dynamic_slice_in_dim(out_gain, place * width, width)

    query_seq, key_seq, value_seq = (moved[i].astype(jnp.float32) for i in range(3))
    grad_rows = moved[3].astype(jnp.float32).reshape(tokens, width)
    attn, back = jax.vjp(
        lambda q, k, v: local_attention(q, k, v, marks, log_decay), query_seq, key_seq, value_seq
    )
    stats = jnp.stack([jnp.sum(attn * attn, axis=-1), jnp.sum(attn * gain * grad_rows, axis=-1)])
    totals = gathered_sum(stats, "seq")
    scale = lax.rsqrt(totals[0] / features + epsilon)[:, None]
    normed = attn * scale * gain
    grad_attn = gain * grad_rows * scale - attn * (scale**3 * (totals[1] / features)[:, None])
    gain_part = jnp.sum(grad_rows * attn * scale, axis=0)
    gain_total = gathered_sum(gain_part, "dp")
    grad_q, grad_k, grad_v = back(grad_attn)

    outs = [part.reshape(count, local_tokens, width).astype(jnp.bfloat16)
            for part in (normed, grad_q, grad_k, grad_v)]
    tail = jnp.zeros((count, 8, width), jnp.bfloat16)
    tail = tail.at[:, :3].set(jnp.broadcast_to(exact_pieces(gain_total)[None], (count, 3, width)))
    returned = lax.all_to_all(jnp.concatenate(outs + [tail], axis=1), "seq", 0, 0, tiled=True)
    span = 4 * local_tokens
    gain_all = jnp.sum(returned[:, span:span + 3].astype(jnp.float32), axis=1).reshape(features)
    results = returned[:, :span].reshape(count, 4, local_tokens, width).transpose(1, 2, 0, 3)
    results = results.reshape(4, 1, local_tokens, features)
    share = features // lax.axis_size("dp")
    grad_gain = lax.dynamic_slice_in_dim(gain_all, lax.axis_index("dp") * share, share)
    return (results[0], results[1], results[2], results[3], grad_gain)


def solution(mesh):
    return jax.shard_map(
        per_device,
        mesh=mesh,
        in_specs=(
            P("dp", "seq", None),
            P("dp", "seq", None),
            P("dp", "seq", None),
            P("dp", "seq"),
            P(),
            P(),
            P("dp", "seq", None),
        ),
        out_specs=(
            P("dp", "seq", None),
            P("dp", "seq", None),
            P("dp", "seq", None),
            P("dp", "seq", None),
            P("dp"),
        ),
        check_vma=False,
    )
```

```python
import jax
import jax.numpy as jnp
from jax import lax
from jax.sharding import PartitionSpec as P

E = 128
CHUNK = 128


highest = lax.Precision.HIGHEST
epsilon = 1e-05


def block_terms(log_decay, marks):
    length = marks.shape[0]
    counted = jnp.cumsum(marks, dtype=jnp.int32)
    places = jnp.arange(length, dtype=jnp.float32)
    offsets = places[:, None] - places[None, :]
    inside = (counted[:, None] == counted[None, :]) & (offsets >= 0.0)
    weights = jnp.where(
        inside[None], jnp.exp2(log_decay[:, None, None] * jnp.maximum(offsets, 0.0)[None]), 0.0
    )
    fresh = (counted == 0).astype(jnp.float32)
    entry = fresh[:, None] * jnp.exp2(log_decay[None, :] * (places[:, None] + 1.0))
    latest = counted[length - 1]
    tail = jnp.where(
        (counted == latest)[:, None],
        jnp.exp2(log_decay[None, :] * (length - 1.0 - places)[:, None]),
        0.0,
    )
    return (weights, entry, tail)


def state_sum(key_block, value_block, tail):
    return jnp.einsum("jhe,jhf->hef", key_block * tail[:, :, None], value_block, precision=highest)


def out_sum(query_block, key_block, value_block, state_in, weights, entry):
    scores = jnp.einsum("ihe,jhe->hij", query_block, key_block, precision=highest) * weights
    inner = jnp.einsum("hij,jhe->ihe", scores, value_block, precision=highest)
    carried = jnp.einsum("ihe,hef->ihf", query_block, state_in, precision=highest)
    return inner + entry[:, :, None] * carried


def chunk_mixing(log_decay, marks, count, length):
    starts = jnp.cumsum(jnp.sum(marks.reshape(count, length), axis=1), dtype=jnp.int32)
    chunk = jnp.arange(count)
    before = jnp.where(chunk >= 1, starts[jnp.maximum(chunk - 1, 0)], 0)
    clear = (chunk[None, :] < chunk[:, None]) & (before[:, None] - starts[None, :] == 0)
    gap = jnp.maximum(chunk[:, None] - chunk[None, :] - 1, 0).astype(jnp.float32)
    return jnp.where(clear[None], jnp.exp2(log_decay[:, None, None] * (length * gap)[None]), 0.0)


def local_attention(query_seq, key_seq, value_seq, marks, log_decay):
    tokens, heads, width = query_seq.shape
    length = CHUNK
    count = tokens // length

    def split(rows):
        return rows.reshape(count, length, heads, width)

    query_blocks, key_blocks, value_blocks = split(query_seq), split(key_seq), split(value_seq)
    weights, entry, tail = jax.vmap(block_terms, (None, 0))(log_decay, marks.reshape(count, length))
    states = jax.vmap(state_sum)(key_blocks, value_blocks, tail)
    mixing = chunk_mixing(log_decay, marks, count, length)
    block_in = jnp.einsum("hcd,dhef->chef", mixing, states, precision=highest)
    outs = jax.vmap(out_sum)(query_blocks, key_blocks, value_blocks, block_in, weights, entry)
    return outs.reshape(tokens, heads * width)


def butterfly_sum(part, axis):
    count = lax.axis_size(axis)
    if count & (count - 1):
        return lax.psum(part, axis)
    distance = 1
    while distance < count:
        part = part + lax.ppermute(part, axis, [(i, i ^ distance) for i in range(count)])
        distance *= 2
    return part


def gathered_sum(part, axis):
    count = lax.axis_size(axis)
    spread = jnp.broadcast_to(part[None], (count,) + part.shape)
    return jnp.sum(lax.all_to_all(spread, axis, 0, 0, tiled=True), axis=0)


def exact_pieces(values):
    pieces = []
    rest = values
    for _ in range(3):
        piece = lax.reduce_precision(rest, exponent_bits=8, mantissa_bits=7)
        pieces.append(piece)
        rest = rest - piece
    return jnp.stack(pieces).astype(jnp.bfloat16)


def per_device(query_rows, key_rows, value_rows, doc_starts, decay_rates, out_gain, cotangent):
    count = lax.axis_size("seq")
    place = lax.axis_index("seq")
    local_tokens, features = query_rows.shape[1], query_rows.shape[2]
    tokens = local_tokens * count
    heads = features // E // count
    width = heads * E
    log_decay = lax.dynamic_slice_in_dim(-decay_rates.astype(jnp.float32) / tokens, place * heads, heads)
    gain = lax.dynamic_slice_in_dim(out_gain, place * width, width)

    mark_rows = local_tokens // width
    extra = -(-max(mark_rows, 1) // 8) * 8
    side = jnp.zeros((count, extra, width), jnp.bfloat16)
    side = side.at[:, :mark_rows].set(
        jnp.broadcast_to(doc_starts[0].astype(jnp.bfloat16).reshape(1, mark_rows, width), (count, mark_rows, width))
    )
    pieces = [rows[0].reshape(local_tokens, count, width).transpose(1, 0, 2)
              for rows in (query_rows, key_rows, value_rows, cotangent)]
    moved = lax.all_to_all(jnp.concatenate(pieces + [side], axis=1), "seq", 0, 0, tiled=True)
    span = 4 * local_tokens
    marks = moved[:, span:span + mark_rows].reshape(tokens).astype(jnp.int32)
    moved = moved[:, :span].reshape(count, 4, local_tokens, heads, E).transpose(1, 0, 2, 3, 4)
    moved = moved.reshape(4, tokens, heads, E)

    query_seq, key_seq, value_seq = (moved[i].astype(jnp.float32) for i in range(3))
    grad_rows = moved[3].astype(jnp.float32).reshape(tokens, width)
    attn, back = jax.vjp(
        lambda q, k, v: local_attention(q, k, v, marks, log_decay), query_seq, key_seq, value_seq
    )
    stats = jnp.stack([jnp.sum(attn * attn, axis=-1), jnp.sum(attn * gain * grad_rows, axis=-1)])
    totals = gathered_sum(stats, "seq")
    scale = lax.rsqrt(totals[0] / features + epsilon)[:, None]
    normed = attn * scale * gain
    grad_attn = gain * grad_rows * scale - attn * (scale**3 * (totals[1] / features)[:, None])
    gain_part = jnp.sum(grad_rows * attn * scale, axis=0)
    grad_q, grad_k, grad_v = back(grad_attn)

    outs = [part.reshape(count, local_tokens, width).astype(jnp.bfloat16)
            for part in (normed, grad_q, grad_k, grad_v)]
    tail = jnp.zeros((count, 8, width), jnp.bfloat16)
    tail = tail.at[:, :3].set(jnp.broadcast_to(exact_pieces(gain_part)[None], (count, 3, width)))
    returned = lax.all_to_all(jnp.concatenate(outs + [tail], axis=1), "seq", 0, 0, tiled=True)
    span = 4 * local_tokens
    gain_all = jnp.sum(returned[:, span:span + 3].astype(jnp.float32), axis=1).reshape(features)
    results = returned[:, :span].reshape(count, 4, local_tokens, width).transpose(1, 2, 0, 3)
    results = results.reshape(4, 1, local_tokens, features)
    groups = lax.axis_size("dp")
    spread = lax.all_to_all(gain_all.reshape(groups, features // groups), "dp", 0, 0, tiled=True)
    grad_gain = jnp.sum(spread, axis=0)
    return (results[0], results[1], results[2], results[3], grad_gain)


def solution(mesh):
    return jax.shard_map(
        per_device,
        mesh=mesh,
        in_specs=(
            P("dp", "seq", None),
            P("dp", "seq", None),
            P("dp", "seq", None),
            P("dp", "seq"),
            P(),
            P(),
            P("dp", "seq", None),
        ),
        out_specs=(
            P("dp", "seq", None),
            P("dp", "seq", None),
            P("dp", "seq", None),
            P("dp", "seq", None),
            P("dp"),
        ),
        check_vma=False,
    )
```

```python
import jax
import jax.numpy as jnp
from jax import lax
from jax.experimental import pallas as pl
from jax.sharding import PartitionSpec as P

E = 128
CHUNK = 128


highest = lax.Precision.HIGHEST
epsilon = 1e-05


def block_terms(log_decay, marks):
    length = marks.shape[0]
    counted = jnp.cumsum(marks, dtype=jnp.int32)
    places = jnp.arange(length, dtype=jnp.float32)
    offsets = places[:, None] - places[None, :]
    inside = (counted[:, None] == counted[None, :]) & (offsets >= 0.0)
    weights = jnp.where(
        inside[None], jnp.exp2(log_decay[:, None, None] * jnp.maximum(offsets, 0.0)[None]), 0.0
    )
    fresh = (counted == 0).astype(jnp.float32)
    entry = fresh[:, None] * jnp.exp2(log_decay[None, :] * (places[:, None] + 1.0))
    latest = counted[length - 1]
    tail = jnp.where(
        (counted == latest)[:, None],
        jnp.exp2(log_decay[None, :] * (length - 1.0 - places)[:, None]),
        0.0,
    )
    return (weights, entry, tail)


def state_sum(key_block, value_block, tail):
    return jnp.einsum("jhe,jhf->hef", key_block * tail[:, :, None], value_block, precision=highest)


def out_sum(query_block, key_block, value_block, state_in, weights, entry):
    scores = jnp.einsum("ihe,jhe->hij", query_block, key_block, precision=highest) * weights
    inner = jnp.einsum("hij,jhe->ihe", scores, value_block, precision=highest)
    carried = jnp.einsum("ihe,hef->ihf", query_block, state_in, precision=highest)
    return inner + entry[:, :, None] * carried


def chunk_mixing(log_decay, marks, count, length):
    starts = jnp.cumsum(jnp.sum(marks.reshape(count, length), axis=1), dtype=jnp.int32)
    chunk = jnp.arange(count)
    before = jnp.where(chunk >= 1, starts[jnp.maximum(chunk - 1, 0)], 0)
    clear = (chunk[None, :] < chunk[:, None]) & (before[:, None] - starts[None, :] == 0)
    gap = jnp.maximum(chunk[:, None] - chunk[None, :] - 1, 0).astype(jnp.float32)
    return jnp.where(clear[None], jnp.exp2(log_decay[:, None, None] * (length * gap)[None]), 0.0)


def local_attention(query_seq, key_seq, value_seq, marks, log_decay):
    tokens, heads, width = query_seq.shape
    length = CHUNK
    count = tokens // length

    def split(rows):
        return rows.reshape(count, length, heads, width)

    query_blocks, key_blocks, value_blocks = split(query_seq), split(key_seq), split(value_seq)
    weights, entry, tail = jax.vmap(block_terms, (None, 0))(log_decay, marks.reshape(count, length))
    states = jax.vmap(state_sum)(key_blocks, value_blocks, tail)
    mixing = chunk_mixing(log_decay, marks, count, length)
    block_in = jnp.einsum("hcd,dhef->chef", mixing, states, precision=highest)
    outs = jax.vmap(out_sum)(query_blocks, key_blocks, value_blocks, block_in, weights, entry)
    return outs.reshape(tokens, heads * width)


def butterfly_sum(part, axis):
    count = lax.axis_size(axis)
    if count & (count - 1):
        return lax.psum(part, axis)
    distance = 1
    while distance < count:
        part = part + lax.ppermute(part, axis, [(i, i ^ distance) for i in range(count)])
        distance *= 2
    return part


def gathered_sum(part, axis):
    count = lax.axis_size(axis)
    spread = jnp.broadcast_to(part[None], (count,) + part.shape)
    return jnp.sum(lax.all_to_all(spread, axis, 0, 0, tiled=True), axis=0)


def exact_pieces(values):
    pieces = []
    rest = values
    for _ in range(3):
        piece = lax.reduce_precision(rest, exponent_bits=8, mantissa_bits=7)
        pieces.append(piece)
        rest = rest - piece
    return jnp.stack(pieces).astype(jnp.bfloat16)


def pack_kernel(query_ref, key_ref, value_ref, grad_ref, marks_ref, out_ref):
    rows = query_ref.shape[1]
    for plane, ref in enumerate((query_ref, key_ref, value_ref, grad_ref)):
        out_ref[0, plane * rows:(plane + 1) * rows, :] = ref[0]
    side = out_ref.shape[1] - 4 * rows
    out_ref[0, 4 * rows:, :] = jnp.zeros((side, out_ref.shape[2]), out_ref.dtype)
    out_ref[0, 4 * rows:4 * rows + 1, :] = marks_ref[...].astype(jnp.float32).astype(out_ref.dtype)


def pack_payload(query_rows, key_rows, value_rows, cotangent, doc_starts, count, width):
    local_tokens = query_rows.shape[1]
    block = pl.BlockSpec((1, local_tokens, width), lambda j: (0, 0, j))
    return pl.pallas_call(
        pack_kernel,
        grid=(count,),
        in_specs=[block, block, block, block, pl.BlockSpec((1, local_tokens), lambda j: (0, 0))],
        out_specs=pl.BlockSpec((1, 4 * local_tokens + 8, width), lambda j: (j, 0, 0)),
        out_shape=jax.ShapeDtypeStruct((count, 4 * local_tokens + 8, width), jnp.bfloat16),
        cost_estimate=pl.CostEstimate(flops=0, transcendentals=0, bytes_accessed=2 * 2 * 4 * local_tokens * width * count),
    )(query_rows, key_rows, value_rows, cotangent, doc_starts)


def per_device(query_rows, key_rows, value_rows, doc_starts, decay_rates, out_gain, cotangent):
    count = lax.axis_size("seq")
    place = lax.axis_index("seq")
    local_tokens, features = query_rows.shape[1], query_rows.shape[2]
    tokens = local_tokens * count
    heads = features // E // count
    width = heads * E
    log_decay = lax.dynamic_slice_in_dim(-decay_rates.astype(jnp.float32) / tokens, place * heads, heads)
    gain = lax.dynamic_slice_in_dim(out_gain, place * width, width)

    mark_rows = 1
    payload = pack_payload(query_rows, key_rows, value_rows, cotangent, doc_starts, count, width)
    moved = lax.all_to_all(payload, "seq", 0, 0, tiled=True)
    span = 4 * local_tokens
    marks = moved[:, span:span + mark_rows].reshape(tokens).astype(jnp.int32)
    moved = moved[:, :span].reshape(count, 4, local_tokens, heads, E).transpose(1, 0, 2, 3, 4)
    moved = moved.reshape(4, tokens, heads, E)

    query_seq, key_seq, value_seq = (moved[i].astype(jnp.float32) for i in range(3))
    grad_rows = moved[3].astype(jnp.float32).reshape(tokens, width)
    attn, back = jax.vjp(
        lambda q, k, v: local_attention(q, k, v, marks, log_decay), query_seq, key_seq, value_seq
    )
    stats = jnp.stack([jnp.sum(attn * attn, axis=-1), jnp.sum(attn * gain * grad_rows, axis=-1)])
    totals = gathered_sum(stats, "seq")
    scale = lax.rsqrt(totals[0] / features + epsilon)[:, None]
    normed = attn * scale * gain
    grad_attn = gain * grad_rows * scale - attn * (scale**3 * (totals[1] / features)[:, None])
    gain_part = jnp.sum(grad_rows * attn * scale, axis=0)
    grad_q, grad_k, grad_v = back(grad_attn)

    outs = [part.reshape(count, local_tokens, width).astype(jnp.bfloat16)
            for part in (normed, grad_q, grad_k, grad_v)]
    tail = jnp.zeros((count, 8, width), jnp.bfloat16)
    tail = tail.at[:, :3].set(jnp.broadcast_to(exact_pieces(gain_part)[None], (count, 3, width)))
    returned = lax.all_to_all(jnp.concatenate(outs + [tail], axis=1), "seq", 0, 0, tiled=True)
    span = 4 * local_tokens
    gain_all = jnp.sum(returned[:, span:span + 3].astype(jnp.float32), axis=1).reshape(features)
    results = returned[:, :span].reshape(count, 4, local_tokens, width).transpose(1, 2, 0, 3)
    results = results.reshape(4, 1, local_tokens, features)
    groups = lax.axis_size("dp")
    spread = lax.all_to_all(gain_all.reshape(groups, features // groups), "dp", 0, 0, tiled=True)
    grad_gain = jnp.sum(spread, axis=0)
    return (results[0], results[1], results[2], results[3], grad_gain)


def solution(mesh):
    return jax.shard_map(
        per_device,
        mesh=mesh,
        in_specs=(
            P("dp", "seq", None),
            P("dp", "seq", None),
            P("dp", "seq", None),
            P("dp", "seq"),
            P(),
            P(),
            P("dp", "seq", None),
        ),
        out_specs=(
            P("dp", "seq", None),
            P("dp", "seq", None),
            P("dp", "seq", None),
            P("dp", "seq", None),
            P("dp"),
        ),
        check_vma=False,
    )
```

```python
import jax
import jax.numpy as jnp
from jax import lax
from jax.experimental import pallas as pl
from jax.sharding import PartitionSpec as P

E = 128
CHUNK = 128


highest = lax.Precision.HIGHEST
epsilon = 1e-05


def block_terms(log_decay, marks):
    length = marks.shape[0]
    counted = jnp.cumsum(marks, dtype=jnp.int32)
    places = jnp.arange(length, dtype=jnp.float32)
    offsets = places[:, None] - places[None, :]
    inside = (counted[:, None] == counted[None, :]) & (offsets >= 0.0)
    weights = jnp.where(
        inside[None], jnp.exp2(log_decay[:, None, None] * jnp.maximum(offsets, 0.0)[None]), 0.0
    )
    fresh = (counted == 0).astype(jnp.float32)
    entry = fresh[:, None] * jnp.exp2(log_decay[None, :] * (places[:, None] + 1.0))
    latest = counted[length - 1]
    tail = jnp.where(
        (counted == latest)[:, None],
        jnp.exp2(log_decay[None, :] * (length - 1.0 - places)[:, None]),
        0.0,
    )
    return (weights, entry, tail)


def state_sum(key_block, value_block, tail):
    return jnp.einsum("jhe,jhf->hef", key_block * tail[:, :, None], value_block, precision=highest)


def out_sum(query_block, key_block, value_block, state_in, weights, entry):
    scores = jnp.einsum("ihe,jhe->hij", query_block, key_block, precision=highest) * weights
    inner = jnp.einsum("hij,jhe->ihe", scores, value_block, precision=highest)
    carried = jnp.einsum("ihe,hef->ihf", query_block, state_in, precision=highest)
    return inner + entry[:, :, None] * carried


def chunk_mixing(log_decay, marks, count, length):
    starts = jnp.cumsum(jnp.sum(marks.reshape(count, length), axis=1), dtype=jnp.int32)
    chunk = jnp.arange(count)
    before = jnp.where(chunk >= 1, starts[jnp.maximum(chunk - 1, 0)], 0)
    clear = (chunk[None, :] < chunk[:, None]) & (before[:, None] - starts[None, :] == 0)
    gap = jnp.maximum(chunk[:, None] - chunk[None, :] - 1, 0).astype(jnp.float32)
    return jnp.where(clear[None], jnp.exp2(log_decay[:, None, None] * (length * gap)[None]), 0.0)


def local_attention(query_seq, key_seq, value_seq, marks, log_decay):
    tokens, heads, width = query_seq.shape
    length = CHUNK
    count = tokens // length

    def split(rows):
        return rows.reshape(count, length, heads, width)

    query_blocks, key_blocks, value_blocks = split(query_seq), split(key_seq), split(value_seq)
    weights, entry, tail = jax.vmap(block_terms, (None, 0))(log_decay, marks.reshape(count, length))
    states = jax.vmap(state_sum)(key_blocks, value_blocks, tail)
    mixing = chunk_mixing(log_decay, marks, count, length)
    block_in = jnp.einsum("hcd,dhef->chef", mixing, states, precision=highest)
    outs = jax.vmap(out_sum)(query_blocks, key_blocks, value_blocks, block_in, weights, entry)
    return outs.reshape(tokens, heads * width)


def butterfly_sum(part, axis):
    count = lax.axis_size(axis)
    if count & (count - 1):
        return lax.psum(part, axis)
    distance = 1
    while distance < count:
        part = part + lax.ppermute(part, axis, [(i, i ^ distance) for i in range(count)])
        distance *= 2
    return part


def gathered_sum(part, axis):
    count = lax.axis_size(axis)
    spread = jnp.broadcast_to(part[None], (count,) + part.shape)
    return jnp.sum(lax.all_to_all(spread, axis, 0, 0, tiled=True), axis=0)


def exact_pieces(values):
    pieces = []
    rest = values
    for _ in range(3):
        piece = lax.reduce_precision(rest, exponent_bits=8, mantissa_bits=7)
        pieces.append(piece)
        rest = rest - piece
    return jnp.stack(pieces).astype(jnp.bfloat16)


def pack_kernel(query_ref, key_ref, value_ref, grad_ref, marks_ref, out_ref):
    rows = query_ref.shape[1]
    group, depth, width = out_ref.shape
    side = depth - 4 * rows
    for dest in range(group):
        columns = slice(dest * width, (dest + 1) * width)
        for plane, ref in enumerate((query_ref, key_ref, value_ref, grad_ref)):
            out_ref[dest, plane * rows:(plane + 1) * rows, :] = ref[0, :, columns]
        out_ref[dest, 4 * rows:, :] = jnp.zeros((side, width), out_ref.dtype)
        out_ref[dest, 4 * rows:4 * rows + 1, :] = marks_ref[...].astype(jnp.float32).astype(out_ref.dtype)


def pack_payload(query_rows, key_rows, value_rows, cotangent, doc_starts, count, width):
    local_tokens = query_rows.shape[1]
    group = 4 if count % 4 == 0 else 1
    block = pl.BlockSpec((1, local_tokens, group * width), lambda j: (0, 0, j))
    return pl.pallas_call(
        pack_kernel,
        grid=(count // group,),
        in_specs=[block, block, block, block, pl.BlockSpec((1, local_tokens), lambda j: (0, 0))],
        out_specs=pl.BlockSpec((group, 4 * local_tokens + 8, width), lambda j: (j, 0, 0)),
        out_shape=jax.ShapeDtypeStruct((count, 4 * local_tokens + 8, width), jnp.bfloat16),
        cost_estimate=pl.CostEstimate(flops=0, transcendentals=0, bytes_accessed=2 * 2 * 4 * local_tokens * width * count),
    )(query_rows, key_rows, value_rows, cotangent, doc_starts)


def per_device(query_rows, key_rows, value_rows, doc_starts, decay_rates, out_gain, cotangent):
    count = lax.axis_size("seq")
    place = lax.axis_index("seq")
    local_tokens, features = query_rows.shape[1], query_rows.shape[2]
    tokens = local_tokens * count
    heads = features // E // count
    width = heads * E
    log_decay = lax.dynamic_slice_in_dim(-decay_rates.astype(jnp.float32) / tokens, place * heads, heads)
    gain = lax.dynamic_slice_in_dim(out_gain, place * width, width)

    mark_rows = 1
    payload = pack_payload(query_rows, key_rows, value_rows, cotangent, doc_starts, count, width)
    moved = lax.all_to_all(payload, "seq", 0, 0, tiled=True)
    span = 4 * local_tokens
    marks = moved[:, span:span + mark_rows].reshape(tokens).astype(jnp.int32)
    moved = moved[:, :span].reshape(count, 4, local_tokens, heads, E).transpose(1, 0, 2, 3, 4)
    moved = moved.reshape(4, tokens, heads, E)

    query_seq, key_seq, value_seq = (moved[i].astype(jnp.float32) for i in range(3))
    grad_rows = moved[3].astype(jnp.float32).reshape(tokens, width)
    attn, back = jax.vjp(
        lambda q, k, v: local_attention(q, k, v, marks, log_decay), query_seq, key_seq, value_seq
    )
    stats = jnp.stack([jnp.sum(attn * attn, axis=-1), jnp.sum(attn * gain * grad_rows, axis=-1)])
    totals = gathered_sum(stats, "seq")
    scale = lax.rsqrt(totals[0] / features + epsilon)[:, None]
    normed = attn * scale * gain
    grad_attn = gain * grad_rows * scale - attn * (scale**3 * (totals[1] / features)[:, None])
    gain_part = jnp.sum(grad_rows * attn * scale, axis=0)
    grad_q, grad_k, grad_v = back(grad_attn)

    outs = [part.reshape(count, local_tokens, width).astype(jnp.bfloat16)
            for part in (normed, grad_q, grad_k, grad_v)]
    tail = jnp.zeros((count, 8, width), jnp.bfloat16)
    tail = tail.at[:, :3].set(jnp.broadcast_to(exact_pieces(gain_part)[None], (count, 3, width)))
    returned = lax.all_to_all(jnp.concatenate(outs + [tail], axis=1), "seq", 0, 0, tiled=True)
    span = 4 * local_tokens
    gain_all = jnp.sum(returned[:, span:span + 3].astype(jnp.float32), axis=1).reshape(features)
    results = returned[:, :span].reshape(count, 4, local_tokens, width).transpose(1, 2, 0, 3)
    results = results.reshape(4, 1, local_tokens, features)
    groups = lax.axis_size("dp")
    spread = lax.all_to_all(gain_all.reshape(groups, features // groups), "dp", 0, 0, tiled=True)
    grad_gain = jnp.sum(spread, axis=0)
    return (results[0], results[1], results[2], results[3], grad_gain)


def solution(mesh):
    return jax.shard_map(
        per_device,
        mesh=mesh,
        in_specs=(
            P("dp", "seq", None),
            P("dp", "seq", None),
            P("dp", "seq", None),
            P("dp", "seq"),
            P(),
            P(),
            P("dp", "seq", None),
        ),
        out_specs=(
            P("dp", "seq", None),
            P("dp", "seq", None),
            P("dp", "seq", None),
            P("dp", "seq", None),
            P("dp"),
        ),
        check_vma=False,
    )
```

```python
import jax
import jax.numpy as jnp
from jax import lax
from jax.experimental import pallas as pl
from jax.sharding import PartitionSpec as P

E = 128
CHUNK = 128


highest = lax.Precision.HIGHEST
epsilon = 1e-05


def block_terms(log_decay, marks):
    length = marks.shape[0]
    counted = jnp.cumsum(marks, dtype=jnp.int32)
    places = jnp.arange(length, dtype=jnp.float32)
    offsets = places[:, None] - places[None, :]
    inside = (counted[:, None] == counted[None, :]) & (offsets >= 0.0)
    weights = jnp.where(
        inside[None], jnp.exp2(log_decay[:, None, None] * jnp.maximum(offsets, 0.0)[None]), 0.0
    )
    fresh = (counted == 0).astype(jnp.float32)
    entry = fresh[:, None] * jnp.exp2(log_decay[None, :] * (places[:, None] + 1.0))
    latest = counted[length - 1]
    tail = jnp.where(
        (counted == latest)[:, None],
        jnp.exp2(log_decay[None, :] * (length - 1.0 - places)[:, None]),
        0.0,
    )
    return (weights, entry, tail)


def state_sum(key_block, value_block, tail):
    return jnp.einsum("jhe,jhf->hef", key_block * tail[:, :, None], value_block, precision=highest)


def out_sum(query_block, key_block, value_block, state_in, weights, entry):
    scores = jnp.einsum("ihe,jhe->hij", query_block, key_block, precision=highest) * weights
    inner = jnp.einsum("hij,jhe->ihe", scores, value_block, precision=highest)
    carried = jnp.einsum("ihe,hef->ihf", query_block, state_in, precision=highest)
    return inner + entry[:, :, None] * carried


def chunk_mixing(log_decay, marks, count, length):
    starts = jnp.cumsum(jnp.sum(marks.reshape(count, length), axis=1), dtype=jnp.int32)
    chunk = jnp.arange(count)
    before = jnp.where(chunk >= 1, starts[jnp.maximum(chunk - 1, 0)], 0)
    clear = (chunk[None, :] < chunk[:, None]) & (before[:, None] - starts[None, :] == 0)
    gap = jnp.maximum(chunk[:, None] - chunk[None, :] - 1, 0).astype(jnp.float32)
    return jnp.where(clear[None], jnp.exp2(log_decay[:, None, None] * (length * gap)[None]), 0.0)


def local_attention(query_seq, key_seq, value_seq, marks, log_decay):
    tokens, heads, width = query_seq.shape
    length = CHUNK
    count = tokens // length

    def split(rows):
        return rows.reshape(count, length, heads, width)

    query_blocks, key_blocks, value_blocks = split(query_seq), split(key_seq), split(value_seq)
    weights, entry, tail = jax.vmap(block_terms, (None, 0))(log_decay, marks.reshape(count, length))
    states = jax.vmap(state_sum)(key_blocks, value_blocks, tail)
    mixing = chunk_mixing(log_decay, marks, count, length)
    block_in = jnp.einsum("hcd,dhef->chef", mixing, states, precision=highest)
    outs = jax.vmap(out_sum)(query_blocks, key_blocks, value_blocks, block_in, weights, entry)
    return outs.reshape(tokens, heads * width)


def butterfly_sum(part, axis):
    count = lax.axis_size(axis)
    if count & (count - 1):
        return lax.psum(part, axis)
    distance = 1
    while distance < count:
        part = part + lax.ppermute(part, axis, [(i, i ^ distance) for i in range(count)])
        distance *= 2
    return part


def gathered_sum(part, axis):
    count = lax.axis_size(axis)
    spread = jnp.broadcast_to(part[None], (count,) + part.shape)
    return jnp.sum(lax.all_to_all(spread, axis, 0, 0, tiled=True), axis=0)


def exact_pieces(values):
    pieces = []
    rest = values
    for _ in range(3):
        piece = lax.reduce_precision(rest, exponent_bits=8, mantissa_bits=7)
        pieces.append(piece)
        rest = rest - piece
    return jnp.stack(pieces).astype(jnp.bfloat16)


def pack_kernel(query_ref, key_ref, value_ref, grad_ref, marks_ref, out_ref):
    rows = query_ref.shape[1]
    group, depth, width = out_ref.shape
    side = depth - 4 * rows
    for dest in range(group):
        columns = slice(dest * width, (dest + 1) * width)
        for plane, ref in enumerate((query_ref, key_ref, value_ref, grad_ref)):
            out_ref[dest, plane * rows:(plane + 1) * rows, :] = ref[0, :, columns]
        out_ref[dest, 4 * rows:, :] = jnp.zeros((side, width), out_ref.dtype)
        out_ref[dest, 4 * rows:4 * rows + 1, :] = marks_ref[...].astype(jnp.float32).astype(out_ref.dtype)


def pack_payload(query_rows, key_rows, value_rows, cotangent, doc_starts, count, width):
    local_tokens = query_rows.shape[1]
    group = 4 if count % 4 == 0 else 1
    block = pl.BlockSpec((1, local_tokens, group * width), lambda j: (0, 0, j))
    return pl.pallas_call(
        pack_kernel,
        grid=(count // group,),
        in_specs=[block, block, block, block, pl.BlockSpec((1, local_tokens), lambda j: (0, 0))],
        out_specs=pl.BlockSpec((group, 4 * local_tokens + 8, width), lambda j: (j, 0, 0)),
        out_shape=jax.ShapeDtypeStruct((count, 4 * local_tokens + 8, width), jnp.bfloat16),
        cost_estimate=pl.CostEstimate(flops=0, transcendentals=0, bytes_accessed=2 * 2 * 4 * local_tokens * width * count),
    )(query_rows, key_rows, value_rows, cotangent, doc_starts)


def per_device(query_rows, key_rows, value_rows, doc_starts, decay_rates, out_gain, cotangent):
    count = lax.axis_size("seq")
    place = lax.axis_index("seq")
    local_tokens, features = query_rows.shape[1], query_rows.shape[2]
    tokens = local_tokens * count
    heads = features // E // count
    width = heads * E
    log_decay = lax.dynamic_slice_in_dim(-decay_rates.astype(jnp.float32) / tokens, place * heads, heads)
    gain = lax.dynamic_slice_in_dim(out_gain, place * width, width)

    mark_rows = 1
    payload = pack_payload(query_rows, key_rows, value_rows, cotangent, doc_starts, count, width)
    moved = lax.all_to_all(payload, "seq", 0, 0, tiled=True)
    span = 4 * local_tokens
    marks = moved[:, span:span + mark_rows].reshape(tokens).astype(jnp.int32)
    moved = moved[:, :span].reshape(count, 4, local_tokens, heads, E).transpose(1, 0, 2, 3, 4)
    moved = moved.reshape(4, tokens, heads, E)

    query_seq, key_seq, value_seq = (moved[i].astype(jnp.float32) for i in range(3))
    grad_rows = moved[3].astype(jnp.float32).reshape(tokens, width)
    attn, back = jax.vjp(
        lambda q, k, v: local_attention(q, k, v, marks, log_decay), query_seq, key_seq, value_seq
    )
    stats = jnp.stack([jnp.sum(attn * attn, axis=-1), jnp.sum(attn * gain * grad_rows, axis=-1)])
    totals = gathered_sum(stats, "seq")
    scale = lax.rsqrt(totals[0] / features + epsilon)[:, None]
    normed = attn * scale * gain
    grad_attn = gain * grad_rows * scale - attn * (scale**3 * (totals[1] / features)[:, None])
    gain_part = jnp.sum(grad_rows * attn * scale, axis=0)
    gain_total = gathered_sum(gain_part, "dp")
    grad_q, grad_k, grad_v = back(grad_attn)

    outs = [part.reshape(count, local_tokens, width).astype(jnp.bfloat16)
            for part in (normed, grad_q, grad_k, grad_v)]
    tail = jnp.zeros((count, 8, width), jnp.bfloat16)
    tail = tail.at[:, :3].set(jnp.broadcast_to(exact_pieces(gain_total)[None], (count, 3, width)))
    share = features // lax.axis_size("dp")
    payload, offset = lax.optimization_barrier((jnp.concatenate(outs + [tail], axis=1), lax.axis_index("dp") * share))
    returned = lax.all_to_all(payload, "seq", 0, 0, tiled=True)
    span = 4 * local_tokens
    gain_all = jnp.sum(returned[:, span:span + 3].astype(jnp.float32), axis=1).reshape(features)
    results = returned[:, :span].reshape(count, 4, local_tokens, width).transpose(1, 2, 0, 3)
    results = results.reshape(4, 1, local_tokens, features)
    grad_gain = lax.dynamic_slice_in_dim(gain_all, offset, share)
    return (results[0], results[1], results[2], results[3], grad_gain)


def solution(mesh):
    return jax.shard_map(
        per_device,
        mesh=mesh,
        in_specs=(
            P("dp", "seq", None),
            P("dp", "seq", None),
            P("dp", "seq", None),
            P("dp", "seq"),
            P(),
            P(),
            P("dp", "seq", None),
        ),
        out_specs=(
            P("dp", "seq", None),
            P("dp", "seq", None),
            P("dp", "seq", None),
            P("dp", "seq", None),
            P("dp"),
        ),
        check_vma=False,
    )
```

```python
import jax
import jax.numpy as jnp
from jax import lax
from jax.experimental import pallas as pl
from jax.sharding import PartitionSpec as P

E = 128
CHUNK = 128


highest = lax.Precision.HIGHEST
epsilon = 1e-05


def block_terms(log_decay, marks):
    length = marks.shape[0]
    counted = jnp.cumsum(marks, dtype=jnp.int32)
    places = jnp.arange(length, dtype=jnp.float32)
    offsets = places[:, None] - places[None, :]
    inside = (counted[:, None] == counted[None, :]) & (offsets >= 0.0)
    weights = jnp.where(
        inside[None], jnp.exp2(log_decay[:, None, None] * jnp.maximum(offsets, 0.0)[None]), 0.0
    )
    fresh = (counted == 0).astype(jnp.float32)
    entry = fresh[:, None] * jnp.exp2(log_decay[None, :] * (places[:, None] + 1.0))
    latest = counted[length - 1]
    tail = jnp.where(
        (counted == latest)[:, None],
        jnp.exp2(log_decay[None, :] * (length - 1.0 - places)[:, None]),
        0.0,
    )
    return (weights, entry, tail)


def state_sum(key_block, value_block, tail):
    return jnp.einsum("jhe,jhf->hef", key_block * tail[:, :, None], value_block, precision=highest)


def out_sum(query_block, key_block, value_block, state_in, weights, entry):
    scores = jnp.einsum("ihe,jhe->hij", query_block, key_block, precision=highest) * weights
    inner = jnp.einsum("hij,jhe->ihe", scores, value_block, precision=highest)
    carried = jnp.einsum("ihe,hef->ihf", query_block, state_in, precision=highest)
    return inner + entry[:, :, None] * carried


def chunk_mixing(log_decay, marks, count, length):
    starts = jnp.cumsum(jnp.sum(marks.reshape(count, length), axis=1), dtype=jnp.int32)
    chunk = jnp.arange(count)
    before = jnp.where(chunk >= 1, starts[jnp.maximum(chunk - 1, 0)], 0)
    clear = (chunk[None, :] < chunk[:, None]) & (before[:, None] - starts[None, :] == 0)
    gap = jnp.maximum(chunk[:, None] - chunk[None, :] - 1, 0).astype(jnp.float32)
    return jnp.where(clear[None], jnp.exp2(log_decay[:, None, None] * (length * gap)[None]), 0.0)


def local_attention(query_seq, key_seq, value_seq, marks, log_decay):
    tokens, heads, width = query_seq.shape
    length = CHUNK
    count = tokens // length

    def split(rows):
        return rows.reshape(count, length, heads, width)

    query_blocks, key_blocks, value_blocks = split(query_seq), split(key_seq), split(value_seq)
    weights, entry, tail = jax.vmap(block_terms, (None, 0))(log_decay, marks.reshape(count, length))
    states = jax.vmap(state_sum)(key_blocks, value_blocks, tail)
    mixing = chunk_mixing(log_decay, marks, count, length)
    block_in = jnp.einsum("hcd,dhef->chef", mixing, states, precision=highest)
    outs = jax.vmap(out_sum)(query_blocks, key_blocks, value_blocks, block_in, weights, entry)
    return outs.reshape(tokens, heads * width)


def butterfly_sum(part, axis):
    count = lax.axis_size(axis)
    if count & (count - 1):
        return lax.psum(part, axis)
    distance = 1
    while distance < count:
        part = part + lax.ppermute(part, axis, [(i, i ^ distance) for i in range(count)])
        distance *= 2
    return part


def gathered_sum(part, axis):
    count = lax.axis_size(axis)
    spread = jnp.broadcast_to(part[None], (count,) + part.shape)
    return jnp.sum(lax.all_to_all(spread, axis, 0, 0, tiled=True), axis=0)


def exact_pieces(values):
    pieces = []
    rest = values
    for _ in range(3):
        piece = lax.reduce_precision(rest, exponent_bits=8, mantissa_bits=7)
        pieces.append(piece)
        rest = rest - piece
    return jnp.stack(pieces).astype(jnp.bfloat16)


def pack_kernel(query_ref, key_ref, value_ref, grad_ref, marks_ref, out_ref):
    rows = query_ref.shape[1]
    group, depth, width = out_ref.shape
    side = depth - 4 * rows
    for dest in range(group):
        columns = slice(dest * width, (dest + 1) * width)
        for plane, ref in enumerate((query_ref, key_ref, value_ref, grad_ref)):
            out_ref[dest, plane * rows:(plane + 1) * rows, :] = ref[0, :, columns]
        out_ref[dest, 4 * rows:, :] = jnp.zeros((side, width), out_ref.dtype)
        out_ref[dest, 4 * rows:4 * rows + 1, :] = marks_ref[...].astype(jnp.float32).astype(out_ref.dtype)


def pack_payload(query_rows, key_rows, value_rows, cotangent, doc_starts, count, width):
    local_tokens = query_rows.shape[1]
    group = 8 if count % 8 == 0 else 1
    block = pl.BlockSpec((1, local_tokens, group * width), lambda j: (0, 0, j))
    return pl.pallas_call(
        pack_kernel,
        grid=(count // group,),
        in_specs=[block, block, block, block, pl.BlockSpec((1, local_tokens), lambda j: (0, 0))],
        out_specs=pl.BlockSpec((group, 4 * local_tokens + 8, width), lambda j: (j, 0, 0)),
        out_shape=jax.ShapeDtypeStruct((count, 4 * local_tokens + 8, width), jnp.bfloat16),
        cost_estimate=pl.CostEstimate(flops=0, transcendentals=0, bytes_accessed=2 * 2 * 4 * local_tokens * width * count),
    )(query_rows, key_rows, value_rows, cotangent, doc_starts)


def per_device(query_rows, key_rows, value_rows, doc_starts, decay_rates, out_gain, cotangent):
    count = lax.axis_size("seq")
    place = lax.axis_index("seq")
    local_tokens, features = query_rows.shape[1], query_rows.shape[2]
    tokens = local_tokens * count
    heads = features // E // count
    width = heads * E
    log_decay = lax.dynamic_slice_in_dim(-decay_rates.astype(jnp.float32) / tokens, place * heads, heads)
    gain = lax.dynamic_slice_in_dim(out_gain, place * width, width)

    mark_rows = 1
    payload = pack_payload(query_rows, key_rows, value_rows, cotangent, doc_starts, count, width)
    moved = lax.all_to_all(payload, "seq", 0, 0, tiled=True)
    span = 4 * local_tokens
    marks = moved[:, span:span + mark_rows].reshape(tokens).astype(jnp.int32)
    moved = moved[:, :span].reshape(count, 4, local_tokens, heads, E).transpose(1, 0, 2, 3, 4)
    moved = moved.reshape(4, tokens, heads, E)

    query_seq, key_seq, value_seq = (moved[i].astype(jnp.float32) for i in range(3))
    grad_rows = moved[3].astype(jnp.float32).reshape(tokens, width)
    attn, back = jax.vjp(
        lambda q, k, v: local_attention(q, k, v, marks, log_decay), query_seq, key_seq, value_seq
    )
    stats = jnp.stack([jnp.sum(attn * attn, axis=-1), jnp.sum(attn * gain * grad_rows, axis=-1)])
    totals = gathered_sum(stats, "seq")
    scale = lax.rsqrt(totals[0] / features + epsilon)[:, None]
    normed = attn * scale * gain
    grad_attn = gain * grad_rows * scale - attn * (scale**3 * (totals[1] / features)[:, None])
    gain_part = jnp.sum(grad_rows * attn * scale, axis=0)
    grad_q, grad_k, grad_v = back(grad_attn)

    outs = [part.reshape(count, local_tokens, width).astype(jnp.bfloat16)
            for part in (normed, grad_q, grad_k, grad_v)]
    tail = jnp.zeros((count, 8, width), jnp.bfloat16)
    tail = tail.at[:, :3].set(jnp.broadcast_to(exact_pieces(gain_part)[None], (count, 3, width)))
    returned = lax.all_to_all(jnp.concatenate(outs + [tail], axis=1), "seq", 0, 0, tiled=True)
    span = 4 * local_tokens
    gain_all = jnp.sum(returned[:, span:span + 3].astype(jnp.float32), axis=1).reshape(features)
    results = returned[:, :span].reshape(count, 4, local_tokens, width).transpose(1, 2, 0, 3)
    results = results.reshape(4, 1, local_tokens, features)
    groups = lax.axis_size("dp")
    spread = lax.all_to_all(gain_all.reshape(groups, features // groups), "dp", 0, 0, tiled=True)
    grad_gain = jnp.sum(spread, axis=0)
    return (results[0], results[1], results[2], results[3], grad_gain)


def solution(mesh):
    return jax.shard_map(
        per_device,
        mesh=mesh,
        in_specs=(
            P("dp", "seq", None),
            P("dp", "seq", None),
            P("dp", "seq", None),
            P("dp", "seq"),
            P(),
            P(),
            P("dp", "seq", None),
        ),
        out_specs=(
            P("dp", "seq", None),
            P("dp", "seq", None),
            P("dp", "seq", None),
            P("dp", "seq", None),
            P("dp"),
        ),
        check_vma=False,
    )
```
